1024 devices in a mesh: dp: 16 (over y, core), expert: 64 (over z, x).
Axes of the slice: x: 4, y: 8, z: 16, core: 2. Of those that a mesh axis runs over, the one named last changes fastest.
Arguments:
- expert_ids: int32 [131072, 4], P(('dp', 'expert')), may hold values from 0 to 63, all different within a row; in each aligned block of 128 rows (0 to 127, 128 to 255, ...) at most 16 rows name the same one
- route_weight: float32 [131072, 4], P(('dp', 'expert')), may hold values from 0.05 to 0.5
- d_gate: bfloat16 [1048576, 768], P(('dp', 'expert')), may hold values from -6 to 6
- gate_weight: bfloat16 [65536, 768], P('expert'), may hold values from -0.21875 to 0.21875
- projector: bfloat16 [1024, 1280], replicated, may hold values from -0.1875 to 0.1875
- enc_pre: bfloat16 [196608, 1280], P(('dp', 'expert')), may hold values from -6 to 6
- span_lengths: int32 [1024, 8], P(('dp', 'expert')), may hold values from 1 to 12, 64 in all within a row
- span_owner: int32 [1024, 8], P(('dp', 'expert')), may hold values from 0 to 15, as said below
- audio_pos: int32 [1024, 64], P(('dp', 'expert')), may hold values from 0 to 127, as said below
Outputs:
- token_grad: bfloat16 [131072, 1024], P(('dp', 'expert'))
- enc_grad: bfloat16 [196608, 1280], P(('dp', 'expert'))
The draws below stay inside these ranges and needn't reach their ends.
Inputs may be any that keep to these rules, and one draw needn't show every extreme that they name: `expert_ids`: each row names 4 different experts; among the rows of one device no expert is named more than 16 times, and some device reaches it. `span_lengths`: each row holds one device's 8 span lengths in order, summing to 64, the largest exactly 12. `span_owner`: the owners of one device's spans are all different. `audio_pos`: each row holds 64 different positions, rising.
All inputs are finite; a program needn't handle non-finite values.
Results may differ from the reference program's by a relative error of at most 0.0064.
Values may be sent and summed in bfloat16 or wider, within the bound.
No kernel may reach another device: no remote copies, remote signals or barrier semaphores. Data moves between devices by JAX's collectives and lax.ppermute only.
A program may use at most 32 MiB of HBM per device.

```python
import math
import jax
import jax.numpy as jnp
import numpy as np
from jax import lax

D = 1024
FFE = 768
EXPERTS = 64
TOP = 4
ENC = 1280
TOK_DEV = 128
NCH = 8
MOSTE = 16
AUD_DEV = 64
CHMOST = 12
TOKENS = 131072
N_DP = 16
N_EXPERT = 64
DEVICES = 1024


def draw_span_owner(key, part):
    scores = jax.random.randint(key, (DEVICES, N_DP), 0, 1 << 20) * N_DP + jnp.arange(N_DP, dtype=jnp.int32)[None, :]
    ordering = jnp.argsort(scores, axis=1, stable=True).astype(jnp.int32)
    return ordering[:, :NCH]


def draw_audio_pos(key, part):
    scores = jax.random.randint(key, (DEVICES, TOK_DEV), 0, 1 << 20) * TOK_DEV + jnp.arange(TOK_DEV, dtype=jnp.int32)[None, :]
    ordering = jnp.argsort(scores, axis=1, stable=True).astype(jnp.int32)
    return jnp.sort(ordering[:, :AUD_DEV], axis=1).astype(jnp.int32)


def level_of(stream_key, dims, cuts, low, high):
    loudness, own = 1.0, jax.random.fold_in(stream_key, 6)
    for axis_at, shards_of in cuts:
        steps = jnp.exp(jax.random.uniform(jax.random.fold_in(own, axis_at), (shards_of,), jnp.float32, low / len(cuts), high / len(cuts)))
        loudness = loudness * jnp.repeat(steps, dims[axis_at] // shards_of).reshape([-1 if axis == axis_at else 1 for axis in range(len(dims))])
    return loudness


def profile(number_of, total, limit, skew):
    weights = [(1 << 20) // math.isqrt(grade ** skew) + 1 for grade in range(2, number_of + 1)]
    rest, holding = total - limit - (number_of - 1), [1] * (number_of - 1)
    while rest > 0:
        free = [i for i in range(number_of - 1) if holding[i] < limit]
        whole, left = sum([weights[i] for i in free]), rest
        for i in free:
            addition = min(limit - holding[i], max(1, left * weights[i] // whole), rest)
            holding[i] = holding[i] + addition
            rest = rest - addition
    return np.array([limit] + holding)


def ragged_sizes(rng, number_of, total, most, lean):
    if number_of == 2:
        one = jax.random.randint(rng, (), max(1, total - most), min(most, total - 1) + 1)
        return jnp.stack([one, total - one])
    tallies = jnp.asarray(profile(number_of, total, most, lean), jnp.int32)
    couples = (number_of - 1) // 2
    source_of, sink = tallies[1:1 + 2 * couples:2], tallies[2:2 + 2 * couples:2]
    slack = jnp.minimum(source_of - 1, most - sink)
    moved = jax.random.randint(jax.random.fold_in(rng, 1), (couples,), 0, 1 << 20) % (slack + 1)
    tallies = tallies.at[1:1 + 2 * couples:2].set(source_of - moved).at[2:2 + 2 * couples:2].set(sink + moved)
    return tallies[jax.random.permutation(jax.random.fold_in(rng, 2), number_of)]


def assign_block(stream_key, own, number, rows, number_of, top, limit, skew):
    order = jax.random.permutation(stream_key, number_of)
    crowded, ordinary = shares(number_of, rows * top, limit, skew, True), shares(number_of, rows * top, limit, skew, False)
    places = jnp.arange(number_of)

    def named(sizes, turn):
        used = int((sizes > 0).sum())
        fixed = max(1, used // 4)
        moved = fixed + (places - fixed + turn * (used - fixed)) % max(1, number_of - fixed)
        return jnp.zeros((number_of,), jnp.int32).at[order[jnp.where(places < fixed, places, moved)]].set(jnp.asarray(sizes, jnp.int32))

    sizes = jnp.where(number % 4 == 0, named(crowded, number // 4), named(ordinary, number - number // 4 - 1))
    mixed = jax.random.permutation(jax.random.fold_in(own, 3), number_of)
    giver, taker = mixed[0:number_of // 2 * 2:2], mixed[1:number_of // 2 * 2:2]
    room = jnp.minimum(sizes[giver] - 1, limit - sizes[taker]) // 2
    room = jnp.where((giver == order[0]) | (taker == order[0]) | (sizes[taker] == 0), 0, jnp.maximum(room, 0))
    moved = jax.random.randint(jax.random.fold_in(own, 4), (number_of // 2,), 0, 1 << 20) % (room + 1)
    sizes = sizes.at[giver].add(-moved).at[taker].add(moved)
    items = jnp.searchsorted(jnp.cumsum(sizes), jnp.arange(rows * top), side="right").astype(jnp.int32)
    grid = items.reshape(top, rows).T
    grid = grid[jax.random.permutation(jax.random.fold_in(own, 1), rows)]
    turn = jax.random.randint(jax.random.fold_in(own, 2), (rows, 1), 0, top)
    return jnp.take_along_axis(grid, (jnp.arange(top)[None, :] + turn) % top, axis=1)


def shares(count, total, most, skew, full):
    weights = [(1 << 20) // math.isqrt(standing ** skew) + 1 for standing in range(1, count + 1)]
    largest = most if full else min(most, max(-(-total // count), total * weights[0] // sum(weights)))
    least = 1 if total - largest >= count - 1 else 0
    given, spare = [largest] + [least] * (count - 1), total - largest - least * (count - 1)
    while spare > 0:
        free = [i for i in range(1, count) if given[i] < largest] or [i for i in range(1, count) if given[i] < most]
        mass, budget = sum([weights[i] for i in free]), spare
        for i in free:
            more = min(most - given[i], max(1, budget * weights[i] // mass), spare)
            given[i] = given[i] + more
            spare = spare - more
    return np.array(given)


def centred(key, extent, deviation, reach, cuts=(), held_as=jnp.bfloat16):
    values = deviation * jax.random.normal(key, extent, jnp.float32)
    if cuts:
        values = values * level_of(key, extent, cuts, -0.22, 0.18)
    return jnp.clip(values, -reach, reach).astype(held_as)


def setup_inputs(seed: int = 0) -> dict:
    streams_of = jax.random.split(jax.random.key(seed), 10)
    expert_ids_keys = jax.random.split(jax.random.fold_in(streams_of[0], 1), TOKENS // TOK_DEV)
    expert_ids_turns = jax.random.permutation(jax.random.fold_in(streams_of[0], 3), TOKENS // TOK_DEV)
    expert_ids = jax.vmap(lambda own, number: assign_block(jax.random.fold_in(streams_of[0], 2), own, number, TOK_DEV, EXPERTS, TOP, MOSTE, 2))(expert_ids_keys, expert_ids_turns).reshape((TOKENS, TOP))
    route_weight = jnp.clip(jnp.exp(math.log(0.5) - 2.3025851 * jax.random.uniform(streams_of[1], (TOKENS, TOP), jnp.float32) ** level_of(streams_of[1], (TOKENS, TOP), ((0, 1024),), -0.2, 0.2)), 0.05, 0.5)
    d_gate = centred(streams_of[2], (DEVICES * EXPERTS * MOSTE, FFE), 1.0, 6.0, ((0, 1024),))
    gate_weight = centred(streams_of[3], (EXPERTS * D, FFE), FFE ** -0.5, 0.21875, ((0, 64),))
    projector = centred(streams_of[4], (D, ENC), D ** -0.5, 0.1875)
    enc_pre = centred(streams_of[5], (DEVICES * N_DP * CHMOST, ENC), 1.5, 6.0, ((0, 1024),))
    span_lengths = jax.vmap(lambda own: ragged_sizes(own, NCH, AUD_DEV, CHMOST, 1))(jax.random.split(streams_of[6], DEVICES)).reshape((DEVICES, NCH)).astype(jnp.int32)
    span_owner = draw_span_owner(jax.random.fold_in(streams_of[9], 71), 0)
    audio_pos = draw_audio_pos(jax.random.fold_in(streams_of[9], 71), 0)
    return dict(expert_ids=expert_ids, route_weight=route_weight, d_gate=d_gate, gate_weight=gate_weight, projector=projector, enc_pre=enc_pre, span_lengths=span_lengths, span_owner=span_owner, audio_pos=audio_pos)


def gelu_slope(values):
    normal_cdf = 0.5 * (1.0 + jax.scipy.special.erf(values * 0.7071067811865476))
    density = jnp.exp(-0.5 * values * values) * 0.3989422804014327
    return normal_cdf + values * density


def route_ranks(id_rows):
    onehot = (id_rows[..., None] == jnp.arange(EXPERTS, dtype=jnp.int32)).astype(jnp.int32)
    counts = jnp.cumsum(onehot, axis=-2)
    return jnp.sum(counts * onehot, axis=-1) - 1


def reference(expert_ids, route_weight, d_gate, gate_weight, projector, enc_pre, span_lengths, span_owner, audio_pos):
    exp_dev = EXPERTS // N_EXPERT
    ranks = route_ranks(expert_ids.reshape(DEVICES, TOK_DEV * TOP)).reshape(TOKENS, TOP)
    grouped = d_gate.reshape(N_DP, N_EXPERT, N_EXPERT, exp_dev, MOSTE, FFE)
    grouped = grouped.transpose(1, 3, 0, 2, 4, 5).reshape(EXPERTS, N_DP * N_EXPERT * MOSTE, FFE)
    weights = gate_weight.reshape(EXPERTS, D, FFE)
    row_base = (jnp.arange(TOKENS, dtype=jnp.int32) // TOK_DEV) * MOSTE

    def visit_expert(total, packed):
        rows_in, weight, expert = packed
        rows_out = jnp.dot(rows_in, weight.T, preferred_element_type=jnp.float32).astype(jnp.bfloat16)
        routed = expert_ids == expert
        share = jnp.sum(jnp.where(routed, route_weight, jnp.zeros_like(route_weight)), axis=1)
        offset = jnp.sum(jnp.where(routed, ranks, jnp.zeros_like(ranks)), axis=1).astype(jnp.int32)
        picked = rows_out[row_base + offset].astype(jnp.float32)
        return total + share[:, None] * picked, None

    start_total = jnp.zeros((TOKENS, D), jnp.float32)
    total, unused = lax.scan(visit_expert, start_total, (grouped, weights, jnp.arange(EXPERTS, dtype=jnp.int32)))
    token_grad = total.astype(jnp.bfloat16)

    device = jnp.arange(DEVICES, dtype=jnp.int32)[:, None]
    audio_rows = token_grad[(device * TOK_DEV + audio_pos).reshape(-1)]
    projected = jnp.dot(audio_rows, projector, preferred_element_type=jnp.float32).astype(jnp.bfloat16)
    starts = (jnp.cumsum(span_lengths, axis=1) - span_lengths).astype(jnp.int32)
    audio_index = jnp.arange(AUD_DEV, dtype=jnp.int32)[None, :]
    span_of = (jnp.sum((audio_index[:, :, None] >= starts[:, None, :]).astype(jnp.int32), axis=2) - 1).astype(jnp.int32)
    offset = audio_index - jnp.take_along_axis(starts, span_of, axis=1)
    owner_of = jnp.take_along_axis(span_owner, span_of, axis=1)
    target = ((owner_of * N_EXPERT + device % N_EXPERT) * N_DP + device // N_EXPERT) * CHMOST + offset
    placed = jnp.zeros((DEVICES * N_DP * CHMOST, ENC), jnp.float32)
    placed = placed.at[target.reshape(-1).astype(jnp.int32)].set(lax.optimization_barrier(projected).astype(jnp.float32))
    enc_grad = (placed * gelu_slope(enc_pre.astype(jnp.float32))).astype(jnp.bfloat16)
    return (token_grad, enc_grad)
```

```python
import jax
import jax.numpy as jnp
from jax import lax
from jax.sharding import Mesh
from jax.sharding import PartitionSpec as P

D = 1024
X_PART = 4


def gelu_slope(values):
    normal_cdf = 0.5 * (1.0 + jax.scipy.special.erf(values * 0.7071067811865476))
    density = jnp.exp(-0.5 * values * values) * 0.3989422804014327
    return normal_cdf + values * density


def body(
    expert_ids,
    route_weight,
    d_gate,
    gate_weight,
    projector,
    enc_pre,
    span_lengths,
    span_owner,
    audio_pos,
):
    nz = lax.axis_size("ez")
    nx = lax.axis_size("ex")
    groups = nz * nx
    exp_dev = gate_weight.shape[0] // D
    experts_all = exp_dev * groups
    capacity_each = d_gate.shape[0] // experts_all
    hidden_width = gate_weight.shape[1]
    column_rows = nx * exp_dev * capacity_each

    incoming = d_gate.reshape(groups, exp_dev, capacity_each, hidden_width)
    weights = gate_weight.reshape(exp_dev, D, hidden_width)
    outgoing = jnp.einsum("sjrf,jdf->sjrd", incoming, weights, preferred_element_type=jnp.float32)
    outgoing = outgoing.astype(jnp.bfloat16).reshape(nz, nx, exp_dev * capacity_each, D)
    got = lax.all_to_all(outgoing, "ex", split_axis=1, concat_axis=1, tiled=True)
    got = got.reshape(nz, column_rows, D)

    token_count, top_count = expert_ids.shape
    flat_ids = expert_ids.reshape(-1)
    onehot = (flat_ids[:, None] == jnp.arange(experts_all, dtype=jnp.int32)[None, :]).astype(
        jnp.int32
    )
    route_rank = jnp.sum(jnp.cumsum(onehot, axis=0) * onehot, axis=1) - 1
    device_of = flat_ids // exp_dev
    column_of = device_of // nx
    row_in_column = ((device_of % nx) * exp_dev + flat_ids % exp_dev) * capacity_each + route_rank
    code = (column_of * column_rows + row_in_column).reshape(token_count, top_count)
    codes = lax.all_gather(code, "ez")
    route_weights = lax.all_gather(route_weight, "ez")

    here = lax.axis_index("ez")
    in_column = codes // column_rows == here
    share = jnp.where(in_column, route_weights, jnp.zeros_like(route_weights))
    picks = (codes % column_rows)[..., None] == jnp.arange(column_rows, dtype=jnp.int32)
    mix = jnp.sum(jnp.where(picks, share[..., None], 0.0), axis=2)
    mix_hi = mix.astype(jnp.bfloat16)
    mix_lo = (mix - mix_hi.astype(jnp.float32)).astype(jnp.bfloat16)
    partial = jnp.einsum("ztr,zrd->ztd", mix_hi, got, preferred_element_type=jnp.float32)
    partial = partial + jnp.einsum("ztr,zrd->ztd", mix_lo, got, preferred_element_type=jnp.float32)
    partial = partial.astype(jnp.bfloat16).reshape(nz * token_count, D)
    token_grad = lax.psum_scatter(partial, "ez", scatter_dimension=0, tiled=True)

    positions = audio_pos[0]
    lengths = span_lengths[0]
    owners = span_owner[0]
    audio_count = positions.shape[0]
    peer_count = lax.axis_size("dp")
    span_cap = enc_pre.shape[0] // peer_count
    starts = jnp.cumsum(lengths) - lengths
    audio_index = jnp.arange(audio_count, dtype=jnp.int32)
    span_of = jnp.sum((audio_index[:, None] >= starts[None, :]).astype(jnp.int32), axis=1) - 1
    offset = audio_index - starts[span_of]
    place_at = owners[span_of] * span_cap + offset
    audio_rows = token_grad[positions]
    parcel = jnp.zeros((peer_count * span_cap, D), jnp.bfloat16).at[place_at].set(audio_rows)
    arrived_rows = lax.all_to_all(
        parcel.reshape(peer_count, span_cap, D), "dp", split_axis=0, concat_axis=0, tiled=True
    )
    arrived_rows = arrived_rows.reshape(peer_count * span_cap, D)
    arrived = jnp.dot(arrived_rows, projector, preferred_element_type=jnp.float32).astype(
        jnp.bfloat16
    )
    gelu_factor = gelu_slope(enc_pre.astype(jnp.float32))
    enc_grad = (lax.optimization_barrier(arrived).astype(jnp.float32) * gelu_factor).astype(
        jnp.bfloat16
    )
    return (token_grad, enc_grad)


def solution(mesh):
    n_dp, n_expert = mesh.devices.shape
    split = Mesh(mesh.devices.reshape(n_dp, n_expert // X_PART, X_PART), ("dp", "ez", "ex"))
    rows = P(("dp", "ez", "ex"), None)
    in_specs = (
        rows,
        rows,
        rows,
        P(("ez", "ex"), None),
        P(),
        rows,
        rows,
        rows,
        rows,
    )
    out_specs = (rows, rows)
    return jax.shard_map(body, mesh=split, in_specs=in_specs, out_specs=out_specs, check_vma=False)
```

```python
import jax
import jax.numpy as jnp
from jax import lax
from jax.sharding import PartitionSpec as P

D = 1024


def gelu_slope(values):
    normal_cdf = 0.5 * (1.0 + jax.scipy.special.erf(values * 0.7071067811865476))
    density = jnp.exp(-0.5 * values * values) * 0.3989422804014327
    return normal_cdf + values * density


def body(
    expert_ids,
    route_weight,
    d_gate,
    gate_weight,
    projector,
    enc_pre,
    span_lengths,
    span_owner,
    audio_pos,
):
    groups = lax.axis_size("expert")
    exp_dev = gate_weight.shape[0] // D
    experts_all = exp_dev * groups
    capacity_each = d_gate.shape[0] // experts_all
    slot_count = exp_dev * capacity_each
    hidden_width = gate_weight.shape[1]
    incoming = d_gate.reshape(groups, exp_dev, capacity_each, hidden_width)
    weights = gate_weight.reshape(exp_dev, D, hidden_width)
    outgoing = jnp.einsum("sjrf,jdf->sjrd", incoming, weights, preferred_element_type=jnp.float32)
    outgoing = outgoing.astype(jnp.bfloat16).reshape(groups, slot_count, D)
    returned = lax.all_to_all(outgoing, "expert", split_axis=0, concat_axis=0, tiled=True)
    returned = returned.reshape(groups * slot_count, D)

    token_count, top_count = expert_ids.shape
    flat_ids = expert_ids.reshape(-1)
    onehot = (flat_ids[:, None] == jnp.arange(experts_all, dtype=jnp.int32)[None, :]).astype(
        jnp.int32
    )
    route_rank = jnp.sum(jnp.cumsum(onehot, axis=0) * onehot, axis=1) - 1
    target = flat_ids // exp_dev * slot_count + flat_ids % exp_dev * capacity_each + route_rank
    slots = jnp.arange(groups * slot_count, dtype=jnp.int32)
    hits = target.reshape(token_count, top_count)[:, :, None] == slots[None, None, :]
    mix = jnp.sum(jnp.where(hits, route_weight[:, :, None], 0.0), axis=1)

    positions = audio_pos[0]
    lengths = span_lengths[0]
    owners = span_owner[0]
    audio_count = positions.shape[0]
    peer_count = lax.axis_size("dp")
    span_cap = enc_pre.shape[0] // peer_count
    starts = jnp.cumsum(lengths) - lengths
    audio_index = jnp.arange(audio_count, dtype=jnp.int32)
    span_of = jnp.sum((audio_index[:, None] >= starts[None, :]).astype(jnp.int32), axis=1) - 1
    offset = audio_index - starts[span_of]
    place_at = owners[span_of] * span_cap + offset
    parcel_rows = jnp.arange(peer_count * span_cap, dtype=jnp.int32)
    lands = place_at[None, :] == parcel_rows[:, None]
    token_of = jnp.sum(jnp.where(lands, positions[None, :] + 1, 0), axis=1) - 1
    parcel_mix = jnp.where((token_of >= 0)[:, None], mix[jnp.maximum(token_of, 0)], 0.0)

    all_mix = jnp.concatenate([mix, parcel_mix], axis=0)
    mix_hi = all_mix.astype(jnp.bfloat16)
    mix_lo = (all_mix - mix_hi.astype(jnp.float32)).astype(jnp.bfloat16)
    summed = jnp.dot(mix_hi, returned, preferred_element_type=jnp.float32)
    summed = summed + jnp.dot(mix_lo, returned, preferred_element_type=jnp.float32)
    summed = summed.astype(jnp.bfloat16)
    token_grad = summed[:token_count]
    parcel = summed[token_count:]

    arrived_rows = lax.all_to_all(
        parcel.reshape(peer_count, span_cap, D), "dp", split_axis=0, concat_axis=0, tiled=True
    )
    arrived_rows = arrived_rows.reshape(peer_count * span_cap, D)
    arrived = jnp.dot(arrived_rows, projector, preferred_element_type=jnp.float32).astype(
        jnp.bfloat16
    )
    gelu_factor = gelu_slope(enc_pre.astype(jnp.float32))
    enc_grad = (lax.optimization_barrier(arrived).astype(jnp.float32) * gelu_factor).astype(
        jnp.bfloat16
    )
    return (token_grad, enc_grad)


def solution(mesh):
    in_specs = (
        P(("dp", "expert"), None),
        P(("dp", "expert"), None),
        P(("dp", "expert"), None),
        P("expert", None),
        P(),
        P(("dp", "expert"), None),
        P(("dp", "expert"), None),
        P(("dp", "expert"), None),
        P(("dp", "expert"), None),
    )
    out_specs = (P(("dp", "expert"), None), P(("dp", "expert"), None))
    return jax.shard_map(body, mesh=mesh, in_specs=in_specs, out_specs=out_specs, check_vma=False)
```

```python
import jax
import jax.numpy as jnp
from jax import lax
from jax.sharding import PartitionSpec as P

D = 1024


def gelu_slope(values):
    normal_cdf = 0.5 * (1.0 + jax.scipy.special.erf(values * 0.7071067811865476))
    density = jnp.exp(-0.5 * values * values) * 0.3989422804014327
    return normal_cdf + values * density


def body(
    expert_ids,
    route_weight,
    d_gate,
    gate_weight,
    projector,
    enc_pre,
    span_lengths,
    span_owner,
    audio_pos,
):
    groups = lax.axis_size("expert")
    exp_dev = gate_weight.shape[0] // D
    experts_all = exp_dev * groups
    capacity_each = d_gate.shape[0] // experts_all
    slot_count = exp_dev * capacity_each
    hidden_width = gate_weight.shape[1]
    incoming = d_gate.reshape(groups, exp_dev, capacity_each, hidden_width)
    weights = gate_weight.reshape(exp_dev, D, hidden_width)
    if exp_dev == 1:
        outgoing = lax.dot_general(
            d_gate, gate_weight, (((1,), (1,)), ((), ())), preferred_element_type=jnp.float32
        )
    else:
        outgoing = jnp.einsum(
            "sjrf,jdf->sjrd", incoming, weights, preferred_element_type=jnp.float32
        )
    outgoing = outgoing.astype(jnp.bfloat16).reshape(groups, slot_count, D)
    returned = lax.all_to_all(outgoing, "expert", split_axis=0, concat_axis=0, tiled=True)
    returned = returned.reshape(groups * slot_count, D)

    token_count, top_count = expert_ids.shape
    flat_ids = expert_ids.reshape(-1)
    onehot = (flat_ids[:, None] == jnp.arange(experts_all, dtype=jnp.int32)[None, :]).astype(
        jnp.int32
    )
    route_rank = jnp.sum(jnp.cumsum(onehot, axis=0) * onehot, axis=1) - 1
    target = flat_ids // exp_dev * slot_count + flat_ids % exp_dev * capacity_each + route_rank
    slots = jnp.arange(groups * slot_count, dtype=jnp.int32)
    hits = target.reshape(token_count, top_count)[:, :, None] == slots[None, None, :]
    mix = jnp.sum(jnp.where(hits, route_weight[:, :, None], 0.0), axis=1)

    positions = audio_pos[0]
    lengths = span_lengths[0]
    owners = span_owner[0]
    audio_count = positions.shape[0]
    peer_count = lax.axis_size("dp")
    span_cap = enc_pre.shape[0] // peer_count
    starts = jnp.cumsum(lengths) - lengths
    audio_index = jnp.arange(audio_count, dtype=jnp.int32)
    span_of = jnp.sum((audio_index[:, None] >= starts[None, :]).astype(jnp.int32), axis=1) - 1
    offset = audio_index - starts[span_of]
    place_at = owners[span_of] * span_cap + offset
    parcel_rows = jnp.arange(peer_count * span_cap, dtype=jnp.int32)
    lands = place_at[None, :] == parcel_rows[:, None]
    token_of = jnp.sum(jnp.where(lands, positions[None, :] + 1, 0), axis=1) - 1
    parcel_mix = jnp.where((token_of >= 0)[:, None], mix[jnp.maximum(token_of, 0)], 0.0)

    def combine(weights_f32):
        hi = lax.optimization_barrier(weights_f32.astype(jnp.bfloat16))
        lo = (weights_f32 - hi.astype(jnp.float32)).astype(jnp.bfloat16)
        total = jnp.dot(hi, returned, preferred_element_type=jnp.float32)
        total = total + jnp.dot(lo, returned, preferred_element_type=jnp.float32)
        return total.astype(jnp.bfloat16)

    parcel = combine(parcel_mix)

    arrived_rows = lax.all_to_all(
        parcel.reshape(peer_count, span_cap, D), "dp", split_axis=0, concat_axis=0, tiled=True
    )
    arrived_rows = arrived_rows.reshape(peer_count * span_cap, D)
    token_grad = combine(mix)
    arrived = jnp.dot(arrived_rows, projector, preferred_element_type=jnp.float32).astype(
        jnp.bfloat16
    )
    gelu_factor = gelu_slope(enc_pre.astype(jnp.float32))
    enc_grad = (lax.optimization_barrier(arrived).astype(jnp.float32) * gelu_factor).astype(
        jnp.bfloat16
    )
    return (token_grad, enc_grad)


def solution(mesh):
    in_specs = (
        P(("dp", "expert"), None),
        P(("dp", "expert"), None),
        P(("dp", "expert"), None),
        P("expert", None),
        P(),
        P(("dp", "expert"), None),
        P(("dp", "expert"), None),
        P(("dp", "expert"), None),
        P(("dp", "expert"), None),
    )
    out_specs = (P(("dp", "expert"), None), P(("dp", "expert"), None))
    return jax.shard_map(body, mesh=mesh, in_specs=in_specs, out_specs=out_specs, check_vma=False)
```

```python
import jax
import jax.numpy as jnp
from jax import lax
from jax.sharding import PartitionSpec as P

D = 1024


def gelu_slope(values):
    normal_cdf = 0.5 * (1.0 + jax.scipy.special.erf(values * 0.7071067811865476))
    density = jnp.exp(-0.5 * values * values) * 0.3989422804014327
    return normal_cdf + values * density


def body(
    expert_ids,
    route_weight,
    d_gate,
    gate_weight,
    projector,
    enc_pre,
    span_lengths,
    span_owner,
    audio_pos,
):
    groups = lax.axis_size("expert")
    exp_dev = gate_weight.shape[0] // D
    experts_all = exp_dev * groups
    capacity_each = d_gate.shape[0] // experts_all
    slot_count = exp_dev * capacity_each
    hidden_width = gate_weight.shape[1]
    incoming = d_gate.reshape(groups, exp_dev, capacity_each, hidden_width)
    weights = gate_weight.reshape(exp_dev, D, hidden_width)
    if exp_dev == 1:
        outgoing = lax.dot_general(
            d_gate, gate_weight, (((1,), (1,)), ((), ())), preferred_element_type=jnp.float32
        )
    else:
        outgoing = jnp.einsum(
            "sjrf,jdf->sjrd", incoming, weights, preferred_element_type=jnp.float32
        )
    outgoing = outgoing.astype(jnp.bfloat16).reshape(groups, slot_count, D)
    returned = lax.all_to_all(outgoing, "expert", split_axis=0, concat_axis=0, tiled=True)
    returned = returned.reshape(groups * slot_count, D)

    token_count, top_count = expert_ids.shape
    flat_ids = expert_ids.reshape(-1)
    onehot = (flat_ids[:, None] == jnp.arange(experts_all, dtype=jnp.int32)[None, :]).astype(
        jnp.int32
    )
    route_rank = jnp.sum(jnp.cumsum(onehot, axis=0) * onehot, axis=1) - 1
    target = flat_ids // exp_dev * slot_count + flat_ids % exp_dev * capacity_each + route_rank
    slots = jnp.arange(groups * slot_count, dtype=jnp.int32)
    hits = target.reshape(token_count, top_count)[:, :, None] == slots[None, None, :]
    mix = jnp.sum(jnp.where(hits, route_weight[:, :, None], 0.0), axis=1)

    positions = audio_pos[0]
    lengths = span_lengths[0]
    owners = span_owner[0]
    audio_count = positions.shape[0]
    peer_count = lax.axis_size("dp")
    span_cap = enc_pre.shape[0] // peer_count
    starts = jnp.cumsum(lengths) - lengths
    audio_index = jnp.arange(audio_count, dtype=jnp.int32)
    span_of = jnp.sum((audio_index[:, None] >= starts[None, :]).astype(jnp.int32), axis=1) - 1
    offset = audio_index - starts[span_of]
    me = lax.axis_index("dp")
    place_at = (owners[span_of] - me) % peer_count * span_cap + offset
    parcel_rows = jnp.arange(peer_count * span_cap, dtype=jnp.int32)
    lands = place_at[None, :] == parcel_rows[:, None]
    token_of = jnp.sum(jnp.where(lands, positions[None, :] + 1, 0), axis=1) - 1
    parcel_mix = jnp.where((token_of >= 0)[:, None], mix[jnp.maximum(token_of, 0)], 0.0)

    def combine(weights_f32):
        hi = lax.optimization_barrier(weights_f32.astype(jnp.bfloat16))
        lo = (weights_f32 - hi.astype(jnp.float32)).astype(jnp.bfloat16)
        total = jnp.dot(hi, returned, preferred_element_type=jnp.float32)
        total = total + jnp.dot(lo, returned, preferred_element_type=jnp.float32)
        return total.astype(jnp.bfloat16)

    parcel = combine(parcel_mix)

    blocks = parcel.reshape(peer_count, span_cap, D)
    got = [blocks[0]]
    for shift in range(1, peer_count):
        pairs = [(i, (i + shift) % peer_count) for i in range(peer_count)]
        got.append(lax.ppermute(blocks[shift], "dp", pairs))
    by_shift = jnp.stack(got)
    senders = (me - jnp.arange(peer_count, dtype=jnp.int32)) % peer_count
    arrived_rows = jnp.take(by_shift, senders, axis=0).reshape(peer_count * span_cap, D)
    token_grad = combine(mix)
    arrived = jnp.dot(arrived_rows, projector, preferred_element_type=jnp.float32).astype(
        jnp.bfloat16
    )
    gelu_factor = gelu_slope(enc_pre.astype(jnp.float32))
    enc_grad = (lax.optimization_barrier(arrived).astype(jnp.float32) * gelu_factor).astype(
        jnp.bfloat16
    )
    return (token_grad, enc_grad)


def solution(mesh):
    in_specs = (
        P(("dp", "expert"), None),
        P(("dp", "expert"), None),
        P(("dp", "expert"), None),
        P("expert", None),
        P(),
        P(("dp", "expert"), None),
        P(("dp", "expert"), None),
        P(("dp", "expert"), None),
        P(("dp", "expert"), None),
    )
    out_specs = (P(("dp", "expert"), None), P(("dp", "expert"), None))
    return jax.shard_map(body, mesh=mesh, in_specs=in_specs, out_specs=out_specs, check_vma=False)
```

```python
import jax
import jax.numpy as jnp
from jax import lax
from jax.sharding import PartitionSpec as P

D = 1024


def gelu_slope(values):
    normal_cdf = 0.5 * (1.0 + jax.scipy.special.erf(values * 0.7071067811865476))
    density = jnp.exp(-0.5 * values * values) * 0.3989422804014327
    return normal_cdf + values * density


def body(
    expert_ids,
    route_weight,
    d_gate,
    gate_weight,
    projector,
    enc_pre,
    span_lengths,
    span_owner,
    audio_pos,
):
    groups = lax.axis_size("expert")
    exp_dev = gate_weight.shape[0] // D
    experts_all = exp_dev * groups
    capacity_each = d_gate.shape[0] // experts_all
    slot_count = exp_dev * capacity_each
    hidden_width = gate_weight.shape[1]
    incoming = d_gate.reshape(groups, exp_dev, capacity_each, hidden_width)
    weights = gate_weight.reshape(exp_dev, D, hidden_width)
    if exp_dev == 1:
        outgoing = lax.dot_general(
            d_gate, gate_weight, (((1,), (1,)), ((), ())), preferred_element_type=jnp.float32
        )
    else:
        outgoing = jnp.einsum(
            "sjrf,jdf->sjrd", incoming, weights, preferred_element_type=jnp.float32
        )
    outgoing = outgoing.astype(jnp.bfloat16).reshape(groups, slot_count, D)
    returned = lax.all_to_all(outgoing, "expert", split_axis=0, concat_axis=0, tiled=True)
    returned = returned.reshape(groups * slot_count, D)

    token_count, top_count = expert_ids.shape
    flat_ids = expert_ids.reshape(-1)
    onehot = (flat_ids[:, None] == jnp.arange(experts_all, dtype=jnp.int32)[None, :]).astype(
        jnp.int32
    )
    route_rank = jnp.sum(jnp.cumsum(onehot, axis=0) * onehot, axis=1) - 1
    target = flat_ids // exp_dev * slot_count + flat_ids % exp_dev * capacity_each + route_rank
    slots = jnp.arange(groups * slot_count, dtype=jnp.int32)
    hits = target.reshape(token_count, top_count)[:, :, None] == slots[None, None, :]
    mix = jnp.sum(jnp.where(hits, route_weight[:, :, None], 0.0), axis=1)

    positions = audio_pos[0]
    lengths = span_lengths[0]
    owners = span_owner[0]
    audio_count = positions.shape[0]
    peer_count = lax.axis_size("dp")
    span_cap = enc_pre.shape[0] // peer_count
    starts = jnp.cumsum(lengths) - lengths
    audio_index = jnp.arange(audio_count, dtype=jnp.int32)
    span_of = jnp.sum((audio_index[:, None] >= starts[None, :]).astype(jnp.int32), axis=1) - 1
    offset = audio_index - starts[span_of]
    block_rows = -(-span_cap // 16) * 16
    place_at = owners[span_of] * block_rows + offset
    parcel_rows = jnp.arange(peer_count * block_rows, dtype=jnp.int32)
    lands = place_at[None, :] == parcel_rows[:, None]
    token_of = jnp.sum(jnp.where(lands, positions[None, :] + 1, 0), axis=1) - 1
    parcel_mix = jnp.where((token_of >= 0)[:, None], mix[jnp.maximum(token_of, 0)], 0.0)

    def combine(weights_f32):
        hi = lax.optimization_barrier(weights_f32.astype(jnp.bfloat16))
        lo = (weights_f32 - hi.astype(jnp.float32)).astype(jnp.bfloat16)
        rows = weights_f32.shape[0]
        total = jnp.dot(jnp.concatenate([hi, lo]), returned, preferred_element_type=jnp.float32)
        return (total[:rows] + total[rows:]).astype(jnp.bfloat16)

    parcel = combine(parcel_mix)

    arrived_rows = lax.all_to_all(
        parcel.reshape(peer_count, block_rows, D), "dp", split_axis=0, concat_axis=0, tiled=True
    )
    arrived_rows = arrived_rows.reshape(peer_count * block_rows, D)
    token_grad = combine(mix)
    arrived = jnp.dot(arrived_rows, projector, preferred_element_type=jnp.float32).astype(
        jnp.bfloat16
    )
    gelu_factor = gelu_slope(enc_pre.astype(jnp.float32))
    arrived = lax.optimization_barrier(arrived).reshape(peer_count, block_rows, -1)
    arrived = arrived[:, :span_cap].reshape(peer_count * span_cap, -1)
    enc_grad = (arrived.astype(jnp.float32) * gelu_factor).astype(jnp.bfloat16)
    return (token_grad, enc_grad)


def solution(mesh):
    in_specs = (
        P(("dp", "expert"), None),
        P(("dp", "expert"), None),
        P(("dp", "expert"), None),
        P("expert", None),
        P(),
        P(("dp", "expert"), None),
        P(("dp", "expert"), None),
        P(("dp", "expert"), None),
        P(("dp", "expert"), None),
    )
    out_specs = (P(("dp", "expert"), None), P(("dp", "expert"), None))
    return jax.shard_map(body, mesh=mesh, in_specs=in_specs, out_specs=out_specs, check_vma=False)
```

```python
import jax
import jax.numpy as jnp
from jax import lax
from jax.sharding import PartitionSpec as P

D = 1024


def gelu_slope(values):
    normal_cdf = 0.5 * (1.0 + jax.scipy.special.erf(values * 0.7071067811865476))
    density = jnp.exp(-0.5 * values * values) * 0.3989422804014327
    return normal_cdf + values * density


def body(
    expert_ids,
    route_weight,
    d_gate,
    gate_weight,
    projector,
    enc_pre,
    span_lengths,
    span_owner,
    audio_pos,
):
    groups = lax.axis_size("expert")
    exp_dev = gate_weight.shape[0] // D
    experts_all = exp_dev * groups
    capacity_each = d_gate.shape[0] // experts_all
    slot_count = exp_dev * capacity_each
    hidden_width = gate_weight.shape[1]
    incoming = d_gate.reshape(groups, exp_dev, capacity_each, hidden_width)
    weights = gate_weight.reshape(exp_dev, D, hidden_width)
    if exp_dev == 1:
        outgoing = lax.dot_general(
            d_gate, gate_weight, (((1,), (1,)), ((), ())), preferred_element_type=jnp.float32
        )
    else:
        outgoing = jnp.einsum(
            "sjrf,jdf->sjrd", incoming, weights, preferred_element_type=jnp.float32
        )
    outgoing = outgoing.astype(jnp.bfloat16).reshape(groups, slot_count, D)
    returned = lax.all_to_all(outgoing, "expert", split_axis=0, concat_axis=0, tiled=True)
    returned = returned.reshape(groups * slot_count, D)

    token_count, top_count = expert_ids.shape
    flat_ids = expert_ids.reshape(-1)
    onehot = (flat_ids[:, None] == jnp.arange(experts_all, dtype=jnp.int32)[None, :]).astype(
        jnp.int32
    )
    route_rank = jnp.sum(jnp.cumsum(onehot, axis=0) * onehot, axis=1) - 1
    target = flat_ids // exp_dev * slot_count + flat_ids % exp_dev * capacity_each + route_rank
    slots = jnp.arange(groups * slot_count, dtype=jnp.int32)
    hits = target.reshape(token_count, top_count)[:, :, None] == slots[None, None, :]
    mix = jnp.sum(jnp.where(hits, route_weight[:, :, None], 0.0), axis=1)

    positions = audio_pos[0]
    lengths = span_lengths[0]
    owners = span_owner[0]
    audio_count = positions.shape[0]
    peer_count = lax.axis_size("dp")
    span_cap = enc_pre.shape[0] // peer_count
    starts = jnp.cumsum(lengths) - lengths
    audio_index = jnp.arange(audio_count, dtype=jnp.int32)
    span_of = jnp.sum((audio_index[:, None] >= starts[None, :]).astype(jnp.int32), axis=1) - 1
    offset = audio_index - starts[span_of]
    place_at = owners[span_of] * span_cap + offset
    parcel_rows = jnp.arange(peer_count * span_cap, dtype=jnp.int32)
    lands = place_at[None, :] == parcel_rows[:, None]
    audio_mix = mix[positions]

    def combine(weights_f32):
        hi = lax.optimization_barrier(weights_f32.astype(jnp.bfloat16))
        lo = (weights_f32 - hi.astype(jnp.float32)).astype(jnp.bfloat16)
        total = jnp.dot(hi, returned, preferred_element_type=jnp.float32)
        total = total + jnp.dot(lo, returned, preferred_element_type=jnp.float32)
        return total.astype(jnp.bfloat16)

    hi = lax.optimization_barrier(audio_mix.astype(jnp.bfloat16))
    lo = (audio_mix - hi.astype(jnp.float32)).astype(jnp.bfloat16)
    both = jnp.dot(jnp.concatenate([hi, lo]), returned, preferred_element_type=jnp.float32)
    audio_rows = (both[:audio_count] + both[audio_count:]).astype(jnp.bfloat16)
    parcel = jnp.dot(lands.astype(jnp.bfloat16), audio_rows, preferred_element_type=jnp.float32)
    parcel = parcel.astype(jnp.bfloat16)

    arrived_rows = lax.all_to_all(
        parcel.reshape(peer_count, span_cap, D), "dp", split_axis=0, concat_axis=0, tiled=True
    )
    arrived_rows = arrived_rows.reshape(peer_count * span_cap, D)
    token_grad = combine(mix)
    arrived = jnp.dot(arrived_rows, projector, preferred_element_type=jnp.float32).astype(
        jnp.bfloat16
    )
    gelu_factor = gelu_slope(enc_pre.astype(jnp.float32))
    enc_grad = (lax.optimization_barrier(arrived).astype(jnp.float32) * gelu_factor).astype(
        jnp.bfloat16
    )
    return (token_grad, enc_grad)


def solution(mesh):
    in_specs = (
        P(("dp", "expert"), None),
        P(("dp", "expert"), None),
        P(("dp", "expert"), None),
        P("expert", None),
        P(),
        P(("dp", "expert"), None),
        P(("dp", "expert"), None),
        P(("dp", "expert"), None),
        P(("dp", "expert"), None),
    )
    out_specs = (P(("dp", "expert"), None), P(("dp", "expert"), None))
    return jax.shard_map(body, mesh=mesh, in_specs=in_specs, out_specs=out_specs, check_vma=False)
```

```python
import jax
import jax.numpy as jnp
from jax import lax
from jax.sharding import PartitionSpec as P

D = 1024


def gelu_slope(values):
    normal_cdf = 0.5 * (1.0 + jax.scipy.special.erf(values * 0.7071067811865476))
    density = jnp.exp(-0.5 * values * values) * 0.3989422804014327
    return normal_cdf + values * density


def body(
    expert_ids,
    route_weight,
    d_gate,
    gate_weight,
    projector,
    enc_pre,
    span_lengths,
    span_owner,
    audio_pos,
):
    groups = lax.axis_size("expert")
    exp_dev = gate_weight.shape[0] // D
    experts_all = exp_dev * groups
    capacity_each = d_gate.shape[0] // experts_all
    slot_count = exp_dev * capacity_each
    hidden_width = gate_weight.shape[1]
    incoming = d_gate.reshape(groups, exp_dev, capacity_each, hidden_width)
    weights = gate_weight.reshape(exp_dev, D, hidden_width)
    if exp_dev == 1:
        outgoing = lax.dot_general(
            d_gate, gate_weight, (((1,), (1,)), ((), ())), preferred_element_type=jnp.float32
        )
    else:
        outgoing = jnp.einsum(
            "sjrf,jdf->sjrd", incoming, weights, preferred_element_type=jnp.float32
        )
    outgoing = outgoing.astype(jnp.bfloat16).reshape(groups, slot_count, D)
    returned = lax.all_to_all(outgoing, "expert", split_axis=0, concat_axis=0, tiled=True)
    returned = returned.reshape(groups * slot_count, D)

    token_count, top_count = expert_ids.shape
    flat_ids = expert_ids.reshape(-1)
    onehot = (flat_ids[:, None] == jnp.arange(experts_all, dtype=jnp.int32)[None, :]).astype(
        jnp.int32
    )
    route_rank = jnp.sum(jnp.cumsum(onehot, axis=0) * onehot, axis=1) - 1
    target = flat_ids // exp_dev * slot_count + flat_ids % exp_dev * capacity_each + route_rank
    slots = jnp.arange(groups * slot_count, dtype=jnp.int32)
    hits = target.reshape(token_count, top_count)[:, :, None] == slots[None, None, :]
    mix = jnp.sum(jnp.where(hits, route_weight[:, :, None], 0.0), axis=1)

    positions = audio_pos[0]
    lengths = span_lengths[0]
    owners = span_owner[0]
    audio_count = positions.shape[0]
    peer_count = lax.axis_size("dp")
    span_cap = enc_pre.shape[0] // peer_count
    starts = jnp.cumsum(lengths) - lengths
    audio_index = jnp.arange(audio_count, dtype=jnp.int32)
    span_of = jnp.sum((audio_index[:, None] >= starts[None, :]).astype(jnp.int32), axis=1) - 1
    offset = audio_index - starts[span_of]
    place_at = owners[span_of] * span_cap + offset
    parcel_rows = jnp.arange(peer_count * span_cap, dtype=jnp.int32)
    lands = place_at[None, :] == parcel_rows[:, None]
    audio_mix = mix[positions]

    def combine(weights_f32):
        hi = lax.optimization_barrier(weights_f32.astype(jnp.bfloat16))
        lo = (weights_f32 - hi.astype(jnp.float32)).astype(jnp.bfloat16)
        total = jnp.dot(hi, returned, preferred_element_type=jnp.float32)
        total = total + jnp.dot(lo, returned, preferred_element_type=jnp.float32)
        return total.astype(jnp.bfloat16)

    hi = lax.optimization_barrier(audio_mix.astype(jnp.bfloat16))
    lo = (audio_mix - hi.astype(jnp.float32)).astype(jnp.bfloat16)
    both = jnp.dot(jnp.concatenate([hi, lo]), returned, preferred_element_type=jnp.float32)
    audio_rows = (both[:audio_count] + both[audio_count:]).astype(jnp.bfloat16)
    parcel = jnp.dot(lands.astype(jnp.bfloat16), audio_rows, preferred_element_type=jnp.float32)
    parcel = parcel.astype(jnp.bfloat16)

    arrived_rows = lax.all_to_all(
        parcel.reshape(peer_count, span_cap, D), "dp", split_axis=0, concat_axis=0, tiled=True
    )
    arrived_rows = arrived_rows.reshape(peer_count * span_cap, D)
    token_grad = combine(mix)
    arrived = jnp.dot(arrived_rows, projector, preferred_element_type=jnp.float32).astype(
        jnp.bfloat16
    )
    gelu_factor = lax.optimization_barrier(gelu_slope(enc_pre.astype(jnp.float32)))
    enc_grad = (arrived.astype(jnp.float32) * gelu_factor).astype(jnp.bfloat16)
    return (token_grad, enc_grad)


def solution(mesh):
    in_specs = (
        P(("dp", "expert"), None),
        P(("dp", "expert"), None),
        P(("dp", "expert"), None),
        P("expert", None),
        P(),
        P(("dp", "expert"), None),
        P(("dp", "expert"), None),
        P(("dp", "expert"), None),
        P(("dp", "expert"), None),
    )
    out_specs = (P(("dp", "expert"), None), P(("dp", "expert"), None))
    return jax.shard_map(body, mesh=mesh, in_specs=in_specs, out_specs=out_specs, check_vma=False)
```

```python
import jax
import jax.numpy as jnp
from jax import lax
from jax.experimental import pallas as pl
from jax.sharding import PartitionSpec as P

D = 1024


def gelu_slope(values):
    normal_cdf = 0.5 * (1.0 + jax.scipy.special.erf(values * 0.7071067811865476))
    density = jnp.exp(-0.5 * values * values) * 0.3989422804014327
    return normal_cdf + values * density


def rows_times_weights_t(rows, weights, block=256):
    count, width = rows.shape
    outs = weights.shape[0]

    def kernel(x_ref, w_ref, o_ref):
        acc = lax.dot_general(
            x_ref[...], w_ref[...], (((1,), (1,)), ((), ())), preferred_element_type=jnp.float32
        )
        o_ref[...] = acc.astype(o_ref.dtype)

    return pl.pallas_call(
        kernel,
        grid=(count // block,),
        in_specs=[
            pl.BlockSpec((block, width), lambda i: (i, 0)),
            pl.BlockSpec((outs, width), lambda i: (0, 0)),
        ],
        out_specs=pl.BlockSpec((block, outs), lambda i: (i, 0)),
        out_shape=jax.ShapeDtypeStruct((count, outs), jnp.bfloat16),
    )(rows, weights)


def body(
    expert_ids,
    route_weight,
    d_gate,
    gate_weight,
    projector,
    enc_pre,
    span_lengths,
    span_owner,
    audio_pos,
):
    groups = lax.axis_size("expert")
    exp_dev = gate_weight.shape[0] // D
    experts_all = exp_dev * groups
    capacity_each = d_gate.shape[0] // experts_all
    slot_count = exp_dev * capacity_each
    hidden_width = gate_weight.shape[1]
    incoming = d_gate.reshape(groups, exp_dev, capacity_each, hidden_width)
    weights = gate_weight.reshape(exp_dev, D, hidden_width)
    if exp_dev == 1 and d_gate.shape[0] % 256 == 0:
        outgoing = rows_times_weights_t(d_gate, gate_weight)
    else:
        outgoing = jnp.einsum(
            "sjrf,jdf->sjrd", incoming, weights, preferred_element_type=jnp.float32
        )
    outgoing = outgoing.astype(jnp.bfloat16).reshape(groups, slot_count, D)
    returned = lax.all_to_all(outgoing, "expert", split_axis=0, concat_axis=0, tiled=True)
    returned = returned.reshape(groups * slot_count, D)

    token_count, top_count = expert_ids.shape
    flat_ids = expert_ids.reshape(-1)
    onehot = (flat_ids[:, None] == jnp.arange(experts_all, dtype=jnp.int32)[None, :]).astype(
        jnp.int32
    )
    route_rank = jnp.sum(jnp.cumsum(onehot, axis=0) * onehot, axis=1) - 1
    target = flat_ids // exp_dev * slot_count + flat_ids % exp_dev * capacity_each + route_rank
    slots = jnp.arange(groups * slot_count, dtype=jnp.int32)
    hits = target.reshape(token_count, top_count)[:, :, None] == slots[None, None, :]
    mix = jnp.sum(jnp.where(hits, route_weight[:, :, None], 0.0), axis=1)

    positions = audio_pos[0]
    lengths = span_lengths[0]
    owners = span_owner[0]
    audio_count = positions.shape[0]
    peer_count = lax.axis_size("dp")
    span_cap = enc_pre.shape[0] // peer_count
    starts = jnp.cumsum(lengths) - lengths
    audio_index = jnp.arange(audio_count, dtype=jnp.int32)
    span_of = jnp.sum((audio_index[:, None] >= starts[None, :]).astype(jnp.int32), axis=1) - 1
    offset = audio_index - starts[span_of]
    place_at = owners[span_of] * span_cap + offset
    parcel_rows = jnp.arange(peer_count * span_cap, dtype=jnp.int32)
    lands = place_at[None, :] == parcel_rows[:, None]
    audio_mix = mix[positions]

    def combine(weights_f32):
        hi = lax.optimization_barrier(weights_f32.astype(jnp.bfloat16))
        lo = (weights_f32 - hi.astype(jnp.float32)).astype(jnp.bfloat16)
        total = jnp.dot(hi, returned, preferred_element_type=jnp.float32)
        total = total + jnp.dot(lo, returned, preferred_element_type=jnp.float32)
        return total.astype(jnp.bfloat16)

    hi = lax.optimization_barrier(audio_mix.astype(jnp.bfloat16))
    lo = (audio_mix - hi.astype(jnp.float32)).astype(jnp.bfloat16)
    both = jnp.dot(jnp.concatenate([hi, lo]), returned, preferred_element_type=jnp.float32)
    audio_rows = (both[:audio_count] + both[audio_count:]).astype(jnp.bfloat16)
    parcel = jnp.dot(lands.astype(jnp.bfloat16), audio_rows, preferred_element_type=jnp.float32)
    parcel = parcel.astype(jnp.bfloat16)

    arrived_rows = lax.all_to_all(
        parcel.reshape(peer_count, span_cap, D), "dp", split_axis=0, concat_axis=0, tiled=True
    )
    arrived_rows = arrived_rows.reshape(peer_count * span_cap, D)
    token_grad = combine(mix)
    arrived = jnp.dot(arrived_rows, projector, preferred_element_type=jnp.float32).astype(
        jnp.bfloat16
    )
    gelu_factor = gelu_slope(enc_pre.astype(jnp.float32))
    enc_grad = (lax.optimization_barrier(arrived).astype(jnp.float32) * gelu_factor).astype(
        jnp.bfloat16
    )
    return (token_grad, enc_grad)


def solution(mesh):
    in_specs = (
        P(("dp", "expert"), None),
        P(("dp", "expert"), None),
        P(("dp", "expert"), None),
        P("expert", None),
        P(),
        P(("dp", "expert"), None),
        P(("dp", "expert"), None),
        P(("dp", "expert"), None),
        P(("dp", "expert"), None),
    )
    out_specs = (P(("dp", "expert"), None), P(("dp", "expert"), None))
    return jax.shard_map(body, mesh=mesh, in_specs=in_specs, out_specs=out_specs, check_vma=False)
```

```python
import jax
import jax.numpy as jnp
from jax import lax
from jax.experimental import pallas as pl
from jax.sharding import PartitionSpec as P

D = 1024


def gelu_slope(values):
    normal_cdf = 0.5 * (1.0 + jax.scipy.special.erf(values * 0.7071067811865476))
    density = jnp.exp(-0.5 * values * values) * 0.3989422804014327
    return normal_cdf + values * density


def audio_parcel(stacked, returned, lands):
    count = stacked.shape[0] // 2
    owners, cap, _ = lands.shape

    def kernel(s_ref, r_ref, l_ref, o_ref):
        both = jnp.dot(s_ref[...], r_ref[...], preferred_element_type=jnp.float32)
        rows = (both[:count] + both[count:]).astype(jnp.bfloat16)
        for owner in range(owners):
            placed = jnp.dot(l_ref[owner], rows, preferred_element_type=jnp.float32)
            o_ref[owner] = placed.astype(o_ref.dtype)

    return pl.pallas_call(
        kernel,
        out_shape=jax.ShapeDtypeStruct((owners, cap, returned.shape[1]), jnp.bfloat16),
    )(stacked, returned, lands)


def body(
    expert_ids,
    route_weight,
    d_gate,
    gate_weight,
    projector,
    enc_pre,
    span_lengths,
    span_owner,
    audio_pos,
):
    groups = lax.axis_size("expert")
    exp_dev = gate_weight.shape[0] // D
    experts_all = exp_dev * groups
    capacity_each = d_gate.shape[0] // experts_all
    slot_count = exp_dev * capacity_each
    hidden_width = gate_weight.shape[1]
    incoming = d_gate.reshape(groups, exp_dev, capacity_each, hidden_width)
    weights = gate_weight.reshape(exp_dev, D, hidden_width)
    if exp_dev == 1:
        outgoing = lax.dot_general(
            d_gate, gate_weight, (((1,), (1,)), ((), ())), preferred_element_type=jnp.float32
        )
    else:
        outgoing = jnp.einsum(
            "sjrf,jdf->sjrd", incoming, weights, preferred_element_type=jnp.float32
        )
    outgoing = outgoing.astype(jnp.bfloat16).reshape(groups, slot_count, D)
    returned = lax.all_to_all(outgoing, "expert", split_axis=0, concat_axis=0, tiled=True)
    returned = returned.reshape(groups * slot_count, D)

    token_count, top_count = expert_ids.shape
    flat_ids = expert_ids.reshape(-1)
    onehot = (flat_ids[:, None] == jnp.arange(experts_all, dtype=jnp.int32)[None, :]).astype(
        jnp.int32
    )
    route_rank = jnp.sum(jnp.cumsum(onehot, axis=0) * onehot, axis=1) - 1
    target = flat_ids // exp_dev * slot_count + flat_ids % exp_dev * capacity_each + route_rank
    slots = jnp.arange(groups * slot_count, dtype=jnp.int32)
    hits = target.reshape(token_count, top_count)[:, :, None] == slots[None, None, :]
    mix = jnp.sum(jnp.where(hits, route_weight[:, :, None], 0.0), axis=1)

    positions = audio_pos[0]
    lengths = span_lengths[0]
    owners = span_owner[0]
    audio_count = positions.shape[0]
    peer_count = lax.axis_size("dp")
    span_cap = enc_pre.shape[0] // peer_count
    starts = jnp.cumsum(lengths) - lengths
    audio_index = jnp.arange(audio_count, dtype=jnp.int32)
    span_of = jnp.sum((audio_index[:, None] >= starts[None, :]).astype(jnp.int32), axis=1) - 1
    offset = audio_index - starts[span_of]
    place_at = owners[span_of] * span_cap + offset
    parcel_rows = jnp.arange(peer_count * span_cap, dtype=jnp.int32)
    lands = place_at[None, :] == parcel_rows[:, None]
    audio_mix = mix[positions]

    def combine(weights_f32):
        hi = lax.optimization_barrier(weights_f32.astype(jnp.bfloat16))
        lo = (weights_f32 - hi.astype(jnp.float32)).astype(jnp.bfloat16)
        total = jnp.dot(hi, returned, preferred_element_type=jnp.float32)
        total = total + jnp.dot(lo, returned, preferred_element_type=jnp.float32)
        return total.astype(jnp.bfloat16)

    hi = lax.optimization_barrier(audio_mix.astype(jnp.bfloat16))
    lo = (audio_mix - hi.astype(jnp.float32)).astype(jnp.bfloat16)
    lands = lands.astype(jnp.bfloat16).reshape(peer_count, span_cap, audio_count)
    parcel = audio_parcel(jnp.concatenate([hi, lo]), returned, lands)

    arrived_rows = lax.all_to_all(parcel, "dp", split_axis=0, concat_axis=0, tiled=True)
    arrived_rows = arrived_rows.reshape(peer_count * span_cap, D)
    token_grad = combine(mix)
    arrived = jnp.dot(arrived_rows, projector, preferred_element_type=jnp.float32).astype(
        jnp.bfloat16
    )
    gelu_factor = gelu_slope(enc_pre.astype(jnp.float32))
    enc_grad = (lax.optimization_barrier(arrived).astype(jnp.float32) * gelu_factor).astype(
        jnp.bfloat16
    )
    return (token_grad, enc_grad)


def solution(mesh):
    in_specs = (
        P(("dp", "expert"), None),
        P(("dp", "expert"), None),
        P(("dp", "expert"), None),
        P("expert", None),
        P(),
        P(("dp", "expert"), None),
        P(("dp", "expert"), None),
        P(("dp", "expert"), None),
        P(("dp", "expert"), None),
    )
    out_specs = (P(("dp", "expert"), None), P(("dp", "expert"), None))
    return jax.shard_map(body, mesh=mesh, in_specs=in_specs, out_specs=out_specs, check_vma=False)
```

```python
import jax
import jax.numpy as jnp
from jax import lax
from jax.experimental import pallas as pl
from jax.sharding import PartitionSpec as P

D = 1024


def gelu_slope(values):
    normal_cdf = 0.5 * (1.0 + jax.scipy.special.erf(values * 0.7071067811865476))
    density = jnp.exp(-0.5 * values * values) * 0.3989422804014327
    return normal_cdf + values * density


def audio_parcel(stacked, returned, lands):
    count = stacked.shape[0] // 2
    owners, cap, _ = lands.shape

    def kernel(s_ref, r_ref, l_ref, o_ref):
        both = jnp.dot(s_ref[...], r_ref[...], preferred_element_type=jnp.float32)
        rows = (both[:count] + both[count:]).astype(jnp.bfloat16)
        for owner in range(owners):
            placed = jnp.dot(l_ref[owner], rows, preferred_element_type=jnp.float32)
            o_ref[owner] = placed.astype(o_ref.dtype)

    return pl.pallas_call(
        kernel,
        out_shape=jax.ShapeDtypeStruct((owners, cap, returned.shape[1]), jnp.bfloat16),
    )(stacked, returned, lands)


def body(
    expert_ids,
    route_weight,
    d_gate,
    gate_weight,
    projector,
    enc_pre,
    span_lengths,
    span_owner,
    audio_pos,
):
    groups = lax.axis_size("expert")
    exp_dev = gate_weight.shape[0] // D
    experts_all = exp_dev * groups
    capacity_each = d_gate.shape[0] // experts_all
    slot_count = exp_dev * capacity_each
    hidden_width = gate_weight.shape[1]
    incoming = d_gate.reshape(groups, exp_dev, capacity_each, hidden_width)
    weights = gate_weight.reshape(exp_dev, D, hidden_width)
    if exp_dev == 1:
        outgoing = lax.dot_general(
            d_gate, gate_weight, (((1,), (1,)), ((), ())), preferred_element_type=jnp.float32
        )
    else:
        outgoing = jnp.einsum(
            "sjrf,jdf->sjrd", incoming, weights, preferred_element_type=jnp.float32
        )
    outgoing = outgoing.astype(jnp.bfloat16).reshape(groups, slot_count, D)
    returned = lax.all_to_all(outgoing, "expert", split_axis=0, concat_axis=0, tiled=True)
    returned = returned.reshape(groups * slot_count, D)

    token_count, top_count = expert_ids.shape
    flat_ids = expert_ids.reshape(-1)
    onehot = (flat_ids[:, None] == jnp.arange(experts_all, dtype=jnp.int32)[None, :]).astype(
        jnp.int32
    )
    route_rank = jnp.sum(jnp.cumsum(onehot, axis=0) * onehot, axis=1) - 1
    target = flat_ids // exp_dev * slot_count + flat_ids % exp_dev * capacity_each + route_rank
    slots = jnp.arange(groups * slot_count, dtype=jnp.int32)
    hits = target.reshape(token_count, top_count)[:, :, None] == slots[None, None, :]
    mix = jnp.sum(jnp.where(hits, route_weight[:, :, None], 0.0), axis=1)

    positions = audio_pos[0]
    lengths = span_lengths[0]
    owners = span_owner[0]
    audio_count = positions.shape[0]
    peer_count = lax.axis_size("dp")
    span_cap = enc_pre.shape[0] // peer_count
    starts = jnp.cumsum(lengths) - lengths
    audio_index = jnp.arange(audio_count, dtype=jnp.int32)
    span_of = jnp.sum((audio_index[:, None] >= starts[None, :]).astype(jnp.int32), axis=1) - 1
    offset = audio_index - starts[span_of]
    place_at = owners[span_of] * span_cap + offset
    parcel_rows = jnp.arange(peer_count * span_cap, dtype=jnp.int32)
    lands = place_at[None, :] == parcel_rows[:, None]
    audio_mix = mix[positions]

    def combine(weights_f32):
        hi = lax.optimization_barrier(weights_f32.astype(jnp.bfloat16))
        lo = (weights_f32 - hi.astype(jnp.float32)).astype(jnp.bfloat16)
        total = jnp.dot(hi, returned, preferred_element_type=jnp.float32)
        total = total + jnp.dot(lo, returned, preferred_element_type=jnp.float32)
        return total.astype(jnp.bfloat16)

    hi = lax.optimization_barrier(audio_mix.astype(jnp.bfloat16))
    lo = (audio_mix - hi.astype(jnp.float32)).astype(jnp.bfloat16)
    lands = lands.astype(jnp.bfloat16).reshape(peer_count, span_cap, audio_count)
    parcel = audio_parcel(jnp.concatenate([hi, lo]), returned, lands)

    arrived_rows = lax.all_to_all(parcel, "dp", split_axis=0, concat_axis=0, tiled=True)
    arrived_rows = arrived_rows.reshape(peer_count * span_cap, D)
    token_grad = combine(mix)
    arrived = jnp.dot(arrived_rows, projector, preferred_element_type=jnp.float32).astype(
        jnp.bfloat16
    )
    gelu_factor = lax.optimization_barrier(gelu_slope(enc_pre.astype(jnp.float32)))
    enc_grad = (arrived.astype(jnp.float32) * gelu_factor).astype(jnp.bfloat16)
    return (token_grad, enc_grad)


def solution(mesh):
    in_specs = (
        P(("dp", "expert"), None),
        P(("dp", "expert"), None),
        P(("dp", "expert"), None),
        P("expert", None),
        P(),
        P(("dp", "expert"), None),
        P(("dp", "expert"), None),
        P(("dp", "expert"), None),
        P(("dp", "expert"), None),
    )
    out_specs = (P(("dp", "expert"), None), P(("dp", "expert"), None))
    return jax.shard_map(body, mesh=mesh, in_specs=in_specs, out_specs=out_specs, check_vma=False)
```
